128 devices in a mesh: wide: 16 (over y, x), narrow: 8 (over z, core).
Axes of the slice: x: 4, y: 4, z: 4, core: 2. Of those that a mesh axis runs over, the one named last changes fastest.
Arguments:
- x_rows: float32 [65536, 256], P('wide'), may hold values from -1.5 to 1.5
- y_cols: float32 [131072, 256], P(('wide', 'narrow')), may hold values from -1.5 to 1.5
- tile_values: bfloat16 [16, 8, 256, 128, 128], P('wide', 'narrow'), may hold values from -6 to 6
- tile_row: int32 [16, 8, 256], P('wide', 'narrow'), may hold values from 0 to 31, as said below
- tile_col: int32 [16, 8, 256], P('wide', 'narrow'), may hold values from 0 to 127
- tile_count: int32 [16, 8], P('wide', 'narrow'), may hold values from 32 to 256, as said below
Outputs:
- x_new: float32 [65536, 256], P('wide')
- y_new: float32 [131072, 256], P(('wide', 'narrow'))
The draws below stay inside these ranges and needn't reach their ends.
Inputs may be any that keep to these rules, and one draw needn't show every extreme that they name: On each device the (tile_row, tile_col) pairs of all 256 slots are distinct. `tile_count`: some device has all 256 slots live.
All inputs are finite; a program needn't handle non-finite values.
Results may differ from the reference program's by a relative error of at most 0.017.
Values may be sent and summed in bfloat16 or wider, within the bound.
No kernel may reach another device: no remote copies, remote signals or barrier semaphores. Data moves between devices by JAX's collectives and lax.ppermute only.
A program may use at most 192 MiB of HBM per device.

```python
import jax
import jax.numpy as jnp
from jax import lax

K = 256
TILE = 128
RB_DEV = 32
CB_DEV = 8
TILES_CAP = 256
ROWS = 65536
COLS = 131072
N_WIDE = 16
N_NARROW = 8


def slot_pairs(key):
    devices_all = N_WIDE * N_NARROW
    keys = jax.random.split(jax.random.fold_in(key, 7), devices_all)
    pairs = RB_DEV * CB_DEV * N_WIDE
    chosen = jax.vmap(lambda k: jax.random.permutation(k, pairs)[:TILES_CAP])(keys)
    return chosen.reshape(N_WIDE, N_NARROW, TILES_CAP).astype(jnp.int32)


def draw_tile_row(key, part):
    return (slot_pairs(key) // (CB_DEV * N_WIDE)).astype(jnp.int32)


def draw_tile_col(key, part):
    return (slot_pairs(key) % (CB_DEV * N_WIDE)).astype(jnp.int32)


def draw_tile_count(key, part):
    devices_all = N_WIDE * N_NARROW
    counts = jax.random.randint(jax.random.fold_in(key, 11), (devices_all,), max(1, TILES_CAP // 8), TILES_CAP + 1)
    fullest = jax.random.randint(jax.random.fold_in(key, 13), (), 0, devices_all)
    counts = counts.at[fullest].set(TILES_CAP)
    return counts.reshape(N_WIDE, N_NARROW).astype(jnp.int32)


def levels(key, shape, cuts, smallest, top_value):
    def one(position, parts):
        steps = jax.random.uniform(jax.random.fold_in(jax.random.fold_in(key, 6), position), (parts,), jnp.float32, smallest / len(cuts), top_value / len(cuts))
        return jnp.repeat(jnp.exp(steps), shape[position] // parts).reshape((-1,) + (1,) * (len(shape) - position - 1))

    gain = one(*cuts[0])
    for cut in cuts[1:]:
        gain = gain * one(*cut)
    return gain


def scatter_about(rng, shape, width, limit, shards=(), kind=jnp.bfloat16):
    entries = width * jax.random.normal(rng, shape, jnp.float32)
    if shards:
        entries = entries * levels(rng, shape, shards, -0.22, 0.18)
    return jnp.clip(entries, -limit, limit).astype(kind)


def setup_inputs(seed: int = 0) -> dict:
    seeds = jax.random.split(jax.random.key(seed), 7)
    x_rows = scatter_about(seeds[0], (ROWS, K), (K ** -0.25), 1.5, ((0, 16),), jnp.float32)
    y_cols = scatter_about(seeds[1], (COLS, K), (K ** -0.25), 1.5, ((0, 128),), jnp.float32)
    tile_values = scatter_about(seeds[2], (N_WIDE, N_NARROW, TILES_CAP, TILE, TILE), 1.0, 6.0, ((0, 16), (1, 8)))
    tile_row = draw_tile_row(jax.random.fold_in(seeds[6], 71), 0)
    tile_col = draw_tile_col(jax.random.fold_in(seeds[6], 71), 0)
    tile_count = draw_tile_count(jax.random.fold_in(seeds[6], 71), 0)
    return {"x_rows": x_rows, "y_cols": y_cols, "tile_values": tile_values, "tile_row": tile_row, "tile_col": tile_col, "tile_count": tile_count}


huber_delta = 1.0
step_rows = 0.008
penalty = 3.0
step_columns = 0.012


def shrink(value, level):
    return jnp.sign(value) * jnp.maximum(jnp.abs(value) - level, 0.0)


def reference(x_rows, y_cols, tile_values, tile_row, tile_col, tile_count):
    total = N_WIDE * N_NARROW * TILES_CAP
    wide_ids = jnp.arange(N_WIDE, dtype=jnp.int32)[:, None, None]
    narrow_ids = jnp.arange(N_NARROW, dtype=jnp.int32)[None, :, None]
    global_rows = (wide_ids * RB_DEV + tile_row).astype(jnp.int32).reshape(total)
    global_cols = (((tile_col // CB_DEV) * N_NARROW + narrow_ids) * CB_DEV + tile_col % CB_DEV).astype(jnp.int32).reshape(total)
    slot_ids = jnp.arange(TILES_CAP, dtype=jnp.int32)[None, None, :]
    live = (slot_ids < tile_count[:, :, None]).astype(jnp.float32).reshape(total)
    groups = total // TILES_CAP
    row_groups = global_rows.reshape(groups, TILES_CAP)
    col_groups = global_cols.reshape(groups, TILES_CAP)
    live_groups = live.reshape(groups, TILES_CAP)
    value_groups = tile_values.reshape(groups, TILES_CAP, TILE, TILE)

    def sweep(x_blocks, y_blocks, want_rows, init):
        def visit(acc, item):
            rows_here, cols_here, live_here, vals = item
            xs = x_blocks[rows_here].astype(jnp.float32)
            ys = y_blocks[cols_here].astype(jnp.float32)
            pred = jnp.einsum('gik,gjk->gij', xs, ys)
            slope = jnp.clip(pred - vals.astype(jnp.float32), -huber_delta, huber_delta) * live_here[:, None, None]
            slope = lax.optimization_barrier(slope.astype(jnp.bfloat16)).astype(jnp.float32)
            if want_rows:
                return acc.at[rows_here].add(jnp.einsum('gij,gjk->gik', slope, ys)), None
            return acc.at[cols_here].add(jnp.einsum('gij,gik->gjk', slope, xs)), None

        result, _ = lax.scan(visit, init, (row_groups, col_groups, live_groups, value_groups))
        return result

    y_blocks = lax.optimization_barrier(y_cols.astype(jnp.bfloat16)).reshape(COLS // TILE, TILE, K)
    x_now = x_rows
    for turn in range(2):
        x_blocks = lax.optimization_barrier(x_now.astype(jnp.bfloat16)).reshape(ROWS // TILE, TILE, K)
        grad_x = sweep(x_blocks, y_blocks, True, jnp.zeros((ROWS // TILE, TILE, K), jnp.float32)).reshape(ROWS, K)
        x_now = shrink(x_now - step_rows * grad_x, step_rows * penalty)
    x_blocks = lax.optimization_barrier(x_now.astype(jnp.bfloat16)).reshape(ROWS // TILE, TILE, K)
    grad_y = sweep(x_blocks, y_blocks, False, jnp.zeros((COLS // TILE, TILE, K), jnp.float32)).reshape(COLS, K)
    return x_now, y_cols - step_columns * grad_y
```

```python
import functools

import jax
import jax.numpy as jnp
from jax import lax
from jax.experimental import pallas as pl
from jax.experimental.pallas import tpu as pltpu
from jax.sharding import PartitionSpec as P

huber_delta = 1.0
step_rows = 0.008
penalty = 3.0
step_columns = 0.012

BATCH = 16
LINK = jnp.bfloat16


def shrink(value, level):
    return jnp.sign(value) * jnp.maximum(jnp.abs(value) - level, 0.0)


def sweep_kernel(want_rows, tile, rows_ref, cols_ref, cnt_ref, x_ref, y_ref, v_ref, out_ref, acc_ref):
    step = pl.program_id(0)
    count = cnt_ref[0]

    @pl.when(step == 0)
    def _():
        acc_ref[...] = jnp.zeros_like(acc_ref)

    def body(j, carry):
        s = step * BATCH + j

        @pl.when(s < count)
        def _():
            r = rows_ref[s]
            c = cols_ref[s]
            r0 = pl.multiple_of(r * tile, tile)
            c0 = pl.multiple_of(c * tile, tile)
            xs = x_ref[pl.ds(r0, tile), :]
            ys = y_ref[pl.ds(c0, tile), :]
            pred = lax.dot_general(xs, ys, (((1,), (1,)), ((), ())), preferred_element_type=jnp.float32)
            vals = v_ref[j].astype(jnp.float32)
            slope = jnp.clip(pred - vals, -huber_delta, huber_delta).astype(jnp.bfloat16)
            if want_rows:
                contrib = jnp.dot(slope, ys, preferred_element_type=jnp.float32)
                acc_ref[pl.ds(r0, tile), :] += contrib
            else:
                contrib = lax.dot_general(slope, xs, (((0,), (0,)), ((), ())), preferred_element_type=jnp.float32)
                acc_ref[pl.ds(c0, tile), :] += contrib

        return carry

    lax.fori_loop(0, BATCH, body, 0)

    @pl.when(step == pl.num_programs(0) - 1)
    def _():
        out_ref[...] = acc_ref[...].astype(out_ref.dtype)


def sweep(want_rows, xb, yb, values, rows_index, cols_index, filled):
    slots, tile, _ = values.shape
    segments = xb.shape[0] if want_rows else yb.shape[0]
    rank = xb.shape[1]
    batches = slots // BATCH

    def v_map(i, rows_ref, cols_ref, cnt_ref):
        last = jnp.maximum(cnt_ref[0] - 1, 0) // BATCH
        return (jnp.minimum(i, last), 0, 0)

    grid_spec = pltpu.PrefetchScalarGridSpec(
        num_scalar_prefetch=3,
        grid=(batches,),
        in_specs=[
            pl.BlockSpec(memory_space=pltpu.VMEM),
            pl.BlockSpec(memory_space=pltpu.VMEM),
            pl.BlockSpec((BATCH, tile, tile), v_map),
        ],
        out_specs=pl.BlockSpec((segments, rank), lambda i, *_: (0, 0)),
        scratch_shapes=[pltpu.VMEM((segments, rank), jnp.float32)],
    )
    flops = 4 * slots * tile * tile * rank
    cost = pl.CostEstimate(
        flops=flops,
        transcendentals=0,
        bytes_accessed=values.size * 2 + xb.size * 2 + yb.size * 2 + segments * rank * 2,
    )
    return pl.pallas_call(
        functools.partial(sweep_kernel, want_rows, tile),
        grid_spec=grid_spec,
        out_shape=jax.ShapeDtypeStruct((segments, rank), LINK),
        compiler_params=pltpu.CompilerParams(
            dimension_semantics=("arbitrary",),
            vmem_limit_bytes=60 * 1024 * 1024,
        ),
        cost_estimate=cost,
    )(rows_index, cols_index, filled, xb, yb, values)


def shards(x_rows, y_cols, tile_values, tile_row, tile_col, tile_count):
    slots = tile_row.shape[-1]
    tile = tile_values.shape[-1]
    yb = lax.all_gather(y_cols.astype(jnp.bfloat16), "wide", axis=0, tiled=True)
    values = tile_values.reshape(slots, tile, tile)
    rows_index = tile_row.reshape(slots)
    cols_index = tile_col.reshape(slots)
    filled = tile_count.reshape(1)

    x_now = x_rows
    for turn in range(2):
        xb = x_now.astype(jnp.bfloat16)
        partial_rows = sweep(True, xb, yb, values, rows_index, cols_index, filled)
        grad_x = lax.psum(partial_rows, "narrow").astype(jnp.float32)
        x_now = shrink(x_now - step_rows * grad_x, step_rows * penalty)
    xb = x_now.astype(jnp.bfloat16)
    partial_cols = sweep(False, xb, yb, values, rows_index, cols_index, filled)
    grad_y = lax.psum_scatter(partial_cols, "wide", scatter_dimension=0, tiled=True).astype(jnp.float32)
    return (x_now, y_cols - step_columns * grad_y)


def solution(mesh):
    placed = (
        P("wide", None),
        P(("wide", "narrow"), None),
        P("wide", "narrow", None, None, None),
        P("wide", "narrow", None),
        P("wide", "narrow", None),
        P("wide", "narrow"),
    )
    return jax.shard_map(
        shards,
        mesh=mesh,
        in_specs=placed,
        out_specs=(P("wide", None), P(("wide", "narrow"), None)),
        check_vma=False,
    )
```

```python
import functools

import jax
import jax.numpy as jnp
from jax import lax
from jax.experimental import pallas as pl
from jax.experimental.pallas import tpu as pltpu
from jax.sharding import PartitionSpec as P

huber_delta = 1.0
step_rows = 0.008
penalty = 3.0
step_columns = 0.012

BATCH = 16


def shrink(value, level):
    return jnp.sign(value) * jnp.maximum(jnp.abs(value) - level, 0.0)


def sweep_kernel(want_rows, tile, rows_ref, cols_ref, cnt_ref, x_ref, y_ref, v_ref, out_ref, acc_ref):
    step = pl.program_id(0)
    count = cnt_ref[0]

    @pl.when(step == 0)
    def _():
        acc_ref[...] = jnp.zeros_like(acc_ref)

    @pl.when(step * BATCH < count)
    def _():
        parts = []
        for j in range(BATCH):
            s = step * BATCH + j
            r0 = pl.multiple_of(rows_ref[s] * tile, tile)
            c0 = pl.multiple_of(cols_ref[s] * tile, tile)
            xs = x_ref[pl.ds(r0, tile), :]
            ys = y_ref[pl.ds(c0, tile), :]
            pred = lax.dot_general(xs, ys, (((1,), (1,)), ((), ())), preferred_element_type=jnp.float32)
            vals = v_ref[j].astype(jnp.float32)
            slope = jnp.where(s < count, jnp.clip(pred - vals, -huber_delta, huber_delta), 0.0).astype(jnp.bfloat16)
            if want_rows:
                parts.append((r0, jnp.dot(slope, ys, preferred_element_type=jnp.float32)))
            else:
                parts.append((c0, lax.dot_general(slope, xs, (((0,), (0,)), ((), ())), preferred_element_type=jnp.float32)))
        for o0, contrib in parts:
            acc_ref[pl.ds(o0, tile), :] += contrib

    @pl.when(step == pl.num_programs(0) - 1)
    def _():
        out_ref[...] = acc_ref[...].astype(out_ref.dtype)


def sweep(want_rows, xb, yb, values, rows_index, cols_index, filled, link):
    slots, tile, _ = values.shape
    segments = xb.shape[0] if want_rows else yb.shape[0]
    rank = xb.shape[1]
    batches = slots // BATCH

    def v_map(i, rows_ref, cols_ref, cnt_ref):
        last = jnp.maximum(cnt_ref[0] - 1, 0) // BATCH
        return (jnp.minimum(i, last), 0, 0)

    grid_spec = pltpu.PrefetchScalarGridSpec(
        num_scalar_prefetch=3,
        grid=(batches,),
        in_specs=[
            pl.BlockSpec(memory_space=pltpu.VMEM),
            pl.BlockSpec(memory_space=pltpu.VMEM),
            pl.BlockSpec((BATCH, tile, tile), v_map),
        ],
        out_specs=pl.BlockSpec((segments, rank), lambda i, *_: (0, 0)),
        scratch_shapes=[pltpu.VMEM((segments, rank), jnp.float32)],
    )
    flops = 4 * slots * tile * tile * rank
    cost = pl.CostEstimate(
        flops=flops,
        transcendentals=0,
        bytes_accessed=values.size * 2 + xb.size * 2 + yb.size * 2 + segments * rank * 2,
    )
    return pl.pallas_call(
        functools.partial(sweep_kernel, want_rows, tile),
        grid_spec=grid_spec,
        out_shape=jax.ShapeDtypeStruct((segments, rank), link),
        compiler_params=pltpu.CompilerParams(
            dimension_semantics=("arbitrary",),
            vmem_limit_bytes=60 * 1024 * 1024,
        ),
        cost_estimate=cost,
    )(rows_index, cols_index, filled, xb, yb, values)


def shards(x_rows, y_cols, tile_values, tile_row, tile_col, tile_count):
    slots = tile_row.shape[-1]
    tile = tile_values.shape[-1]
    yb = lax.all_gather(y_cols.astype(jnp.bfloat16), "wide", axis=0, tiled=True)
    values = tile_values.reshape(slots, tile, tile)
    rows_index = tile_row.reshape(slots)
    cols_index = tile_col.reshape(slots)
    filled = tile_count.reshape(1)

    x_now = x_rows
    for turn in range(2):
        xb = x_now.astype(jnp.bfloat16)
        partial_rows = sweep(True, xb, yb, values, rows_index, cols_index, filled, jnp.float32)
        grad_x = lax.psum(partial_rows, "narrow")
        x_now = shrink(x_now - step_rows * grad_x, step_rows * penalty)
    xb = x_now.astype(jnp.bfloat16)
    partial_cols = sweep(False, xb, yb, values, rows_index, cols_index, filled, jnp.bfloat16)
    grad_y = lax.psum_scatter(partial_cols, "wide", scatter_dimension=0, tiled=True).astype(jnp.float32)
    return (x_now, y_cols - step_columns * grad_y)


def solution(mesh):
    placed = (
        P("wide", None),
        P(("wide", "narrow"), None),
        P("wide", "narrow", None, None, None),
        P("wide", "narrow", None),
        P("wide", "narrow", None),
        P("wide", "narrow"),
    )
    return jax.shard_map(
        shards,
        mesh=mesh,
        in_specs=placed,
        out_specs=(P("wide", None), P(("wide", "narrow"), None)),
        check_vma=False,
    )
```

```python
import functools

import jax
import jax.numpy as jnp
from jax import lax
from jax.experimental import pallas as pl
from jax.experimental.pallas import tpu as pltpu
from jax.sharding import PartitionSpec as P

huber_delta = 1.0
step_rows = 0.008
penalty = 3.0
step_columns = 0.012

BATCH = 16


def shrink(value, level):
    return jnp.sign(value) * jnp.maximum(jnp.abs(value) - level, 0.0)


def sweep_kernel(want_rows, tile, rows_ref, cols_ref, cnt_ref, x_ref, y_ref, v_ref, out_ref, acc_ref):
    step = pl.program_id(0)
    count = cnt_ref[0]

    @pl.when(step == 0)
    def _():
        acc_ref[...] = jnp.zeros_like(acc_ref)

    @pl.when(step * BATCH < count)
    def _():
        parts = []
        for j in range(BATCH):
            s = step * BATCH + j
            r0 = pl.multiple_of(rows_ref[s] * tile, tile)
            c0 = pl.multiple_of(cols_ref[s] * tile, tile)
            xs = x_ref[pl.ds(r0, tile), :].astype(jnp.bfloat16)
            ys = y_ref[pl.ds(c0, tile), :]
            pred = lax.dot_general(xs, ys, (((1,), (1,)), ((), ())), preferred_element_type=jnp.float32)
            vals = v_ref[j].astype(jnp.float32)
            slope = jnp.where(s < count, jnp.clip(pred - vals, -huber_delta, huber_delta), 0.0).astype(jnp.bfloat16)
            if want_rows:
                parts.append((r0, jnp.dot(slope, ys, preferred_element_type=jnp.float32)))
            else:
                parts.append((c0, lax.dot_general(slope, xs, (((0,), (0,)), ((), ())), preferred_element_type=jnp.float32)))
        for o0, contrib in parts:
            acc_ref[pl.ds(o0, tile), :] += contrib

    @pl.when(step == pl.num_programs(0) - 1)
    def _():
        out_ref[...] = acc_ref[...].astype(out_ref.dtype)


def sweep(want_rows, xb, yb, values, rows_index, cols_index, filled, link):
    slots, tile, _ = values.shape
    segments = xb.shape[0] if want_rows else yb.shape[0]
    rank = xb.shape[1]
    batches = slots // BATCH

    def v_map(i, rows_ref, cols_ref, cnt_ref):
        last = jnp.maximum(cnt_ref[0] - 1, 0) // BATCH
        return (jnp.minimum(i, last), 0, 0)

    grid_spec = pltpu.PrefetchScalarGridSpec(
        num_scalar_prefetch=3,
        grid=(batches,),
        in_specs=[
            pl.BlockSpec(memory_space=pltpu.VMEM),
            pl.BlockSpec(memory_space=pltpu.VMEM),
            pl.BlockSpec((BATCH, tile, tile), v_map),
        ],
        out_specs=pl.BlockSpec((segments, rank), lambda i, *_: (0, 0)),
        scratch_shapes=[pltpu.VMEM((segments, rank), jnp.float32)],
    )
    flops = 4 * slots * tile * tile * rank
    cost = pl.CostEstimate(
        flops=flops,
        transcendentals=0,
        bytes_accessed=values.size * 2 + xb.size * xb.dtype.itemsize + yb.size * 2 + segments * rank * 2,
    )
    return pl.pallas_call(
        functools.partial(sweep_kernel, want_rows, tile),
        grid_spec=grid_spec,
        out_shape=jax.ShapeDtypeStruct((segments, rank), link),
        compiler_params=pltpu.CompilerParams(
            dimension_semantics=("arbitrary",),
            vmem_limit_bytes=60 * 1024 * 1024,
        ),
        cost_estimate=cost,
    )(rows_index, cols_index, filled, xb, yb, values)


def shards(x_rows, y_cols, tile_values, tile_row, tile_col, tile_count):
    slots = tile_row.shape[-1]
    tile = tile_values.shape[-1]
    yb = lax.all_gather(y_cols.astype(jnp.bfloat16), "wide", axis=0, tiled=True)
    values = tile_values.reshape(slots, tile, tile)
    rows_index = tile_row.reshape(slots)
    cols_index = tile_col.reshape(slots)
    filled = tile_count.reshape(1)

    rows_here = x_rows.shape[0] // lax.axis_size("narrow")
    first = lax.axis_index("narrow") * rows_here
    level = step_rows * penalty

    partial_rows = sweep(True, x_rows.astype(jnp.bfloat16), yb, values, rows_index, cols_index, filled, jnp.float32)
    grad_x = lax.psum_scatter(partial_rows, "narrow", scatter_dimension=0, tiled=True)
    x_mine = shrink(lax.dynamic_slice_in_dim(x_rows, first, rows_here, 0) - step_rows * grad_x, level)
    xb = lax.all_gather(x_mine.astype(jnp.bfloat16), "narrow", axis=0, tiled=True)

    partial_rows = sweep(True, xb, yb, values, rows_index, cols_index, filled, jnp.float32)
    grad_x = lax.psum_scatter(partial_rows, "narrow", scatter_dimension=0, tiled=True)
    x_mine = shrink(x_mine - step_rows * grad_x, level)
    x_now = lax.all_gather(x_mine, "narrow", axis=0, tiled=True)

    partial_cols = sweep(False, x_now, yb, values, rows_index, cols_index, filled, jnp.bfloat16)
    grad_y = lax.psum_scatter(partial_cols, "wide", scatter_dimension=0, tiled=True).astype(jnp.float32)
    return (x_now, y_cols - step_columns * grad_y)


def solution(mesh):
    placed = (
        P("wide", None),
        P(("wide", "narrow"), None),
        P("wide", "narrow", None, None, None),
        P("wide", "narrow", None),
        P("wide", "narrow", None),
        P("wide", "narrow"),
    )
    return jax.shard_map(
        shards,
        mesh=mesh,
        in_specs=placed,
        out_specs=(P("wide", None), P(("wide", "narrow"), None)),
        check_vma=False,
    )
```

```python
import functools

import jax
import jax.numpy as jnp
from jax import lax
from jax.experimental import pallas as pl
from jax.experimental.pallas import tpu as pltpu
from jax.sharding import PartitionSpec as P

huber_delta = 1.0
step_rows = 0.008
penalty = 3.0
step_columns = 0.012

BATCH = 32


def shrink(value, level):
    return jnp.sign(value) * jnp.maximum(jnp.abs(value) - level, 0.0)


def sweep_kernel(want_rows, tile, rows_ref, cols_ref, cnt_ref, x_ref, y_ref, v_ref, out_ref, *rest):
    acc_ref = rest[-1]
    step = pl.program_id(0)
    count = cnt_ref[0]

    @pl.when(step == 0)
    def _():
        acc_ref[...] = jnp.zeros_like(acc_ref)
        if len(rest) > 1:
            rest[0][...] = x_ref[...]

    @pl.when(step * BATCH < count)
    def _():
        parts = []
        for j in range(BATCH):
            s = step * BATCH + j
            r0 = pl.multiple_of(rows_ref[s] * tile, tile)
            c0 = pl.multiple_of(cols_ref[s] * tile, tile)
            xs = x_ref[pl.ds(r0, tile), :].astype(jnp.bfloat16)
            ys = y_ref[pl.ds(c0, tile), :]
            pred = lax.dot_general(xs, ys, (((1,), (1,)), ((), ())), preferred_element_type=jnp.float32)
            vals = v_ref[j].astype(jnp.float32)
            slope = jnp.where(s < count, jnp.clip(pred - vals, -huber_delta, huber_delta), 0.0).astype(jnp.bfloat16)
            if want_rows:
                parts.append((r0, jnp.dot(slope, ys, preferred_element_type=jnp.float32)))
            else:
                parts.append((c0, lax.dot_general(slope, xs, (((0,), (0,)), ((), ())), preferred_element_type=jnp.float32)))
        for o0, contrib in parts:
            acc_ref[pl.ds(o0, tile), :] += contrib

    @pl.when(step == pl.num_programs(0) - 1)
    def _():
        out_ref[...] = acc_ref[...].astype(out_ref.dtype)


def sweep(want_rows, xb, yb, values, rows_index, cols_index, filled, link, echo=False):
    slots, tile, _ = values.shape
    segments = xb.shape[0] if want_rows else yb.shape[0]
    rank = xb.shape[1]
    batches = slots // BATCH

    def v_map(i, rows_ref, cols_ref, cnt_ref):
        last = jnp.maximum(cnt_ref[0] - 1, 0) // BATCH
        return (jnp.minimum(i, last), 0, 0)

    grid_spec = pltpu.PrefetchScalarGridSpec(
        num_scalar_prefetch=3,
        grid=(batches,),
        in_specs=[
            pl.BlockSpec(memory_space=pltpu.VMEM),
            pl.BlockSpec(memory_space=pltpu.VMEM),
            pl.BlockSpec((BATCH, tile, tile), v_map),
        ],
        out_specs=[pl.BlockSpec((segments, rank), lambda i, *_: (0, 0))]
        + ([pl.BlockSpec(xb.shape, lambda i, *_: (0, 0))] if echo else []),
        scratch_shapes=[pltpu.VMEM((segments, rank), jnp.float32)],
    )
    flops = 4 * slots * tile * tile * rank
    cost = pl.CostEstimate(
        flops=flops,
        transcendentals=0,
        bytes_accessed=values.size * 2 + xb.size * xb.dtype.itemsize + yb.size * 2 + segments * rank * 2,
    )
    outs = pl.pallas_call(
        functools.partial(sweep_kernel, want_rows, tile),
        grid_spec=grid_spec,
        out_shape=[jax.ShapeDtypeStruct((segments, rank), link)]
        + ([jax.ShapeDtypeStruct(xb.shape, xb.dtype)] if echo else []),
        compiler_params=pltpu.CompilerParams(
            dimension_semantics=("arbitrary",),
            vmem_limit_bytes=60 * 1024 * 1024,
        ),
        cost_estimate=cost,
    )(rows_index, cols_index, filled, xb, yb, values)
    return outs if echo else outs[0]


def shards(x_rows, y_cols, tile_values, tile_row, tile_col, tile_count):
    slots = tile_row.shape[-1]
    tile = tile_values.shape[-1]
    yb = lax.all_gather(y_cols.astype(jnp.bfloat16), "wide", axis=0, tiled=True)
    values = tile_values.reshape(slots, tile, tile)
    rows_index = tile_row.reshape(slots)
    cols_index = tile_col.reshape(slots)
    filled = tile_count.reshape(1)

    rows_here = x_rows.shape[0] // lax.axis_size("narrow")
    first = lax.axis_index("narrow") * rows_here
    level = step_rows * penalty

    partial_rows = sweep(True, x_rows.astype(jnp.bfloat16), yb, values, rows_index, cols_index, filled, jnp.float32)
    grad_x = lax.psum_scatter(partial_rows, "narrow", scatter_dimension=0, tiled=True)
    x_mine = shrink(lax.dynamic_slice_in_dim(x_rows, first, rows_here, 0) - step_rows * grad_x, level)
    xb = lax.all_gather(x_mine.astype(jnp.bfloat16), "narrow", axis=0, tiled=True)

    partial_rows = sweep(True, xb, yb, values, rows_index, cols_index, filled, jnp.float32)
    grad_x = lax.psum_scatter(partial_rows, "narrow", scatter_dimension=0, tiled=True)
    x_mine = shrink(x_mine - step_rows * grad_x, level)
    x_now = lax.all_gather(x_mine, "narrow", axis=0, tiled=True)

    partial_cols, x_out = sweep(False, x_now, yb, values, rows_index, cols_index, filled, jnp.bfloat16, echo=True)
    grad_y = lax.psum_scatter(partial_cols, "wide", scatter_dimension=0, tiled=True).astype(jnp.float32)
    return (x_out, y_cols - step_columns * grad_y)


def solution(mesh):
    placed = (
        P("wide", None),
        P(("wide", "narrow"), None),
        P("wide", "narrow", None, None, None),
        P("wide", "narrow", None),
        P("wide", "narrow", None),
        P("wide", "narrow"),
    )
    return jax.shard_map(
        shards,
        mesh=mesh,
        in_specs=placed,
        out_specs=(P("wide", None), P(("wide", "narrow"), None)),
        check_vma=False,
    )
```

```python
import functools

import jax
import jax.numpy as jnp
from jax import lax
from jax.experimental import pallas as pl
from jax.experimental.pallas import tpu as pltpu
from jax.sharding import PartitionSpec as P

huber_delta = 1.0
step_rows = 0.008
penalty = 3.0
step_columns = 0.012

BATCH = 64


def shrink(value, level):
    return jnp.sign(value) * jnp.maximum(jnp.abs(value) - level, 0.0)


def sweep_kernel(want_rows, tile, rows_ref, cols_ref, cnt_ref, x_ref, y_ref, v_ref, out_ref, acc_ref):
    step = pl.program_id(0)
    count = cnt_ref[0]

    @pl.when(step == 0)
    def _():
        acc_ref[...] = jnp.zeros_like(acc_ref)

    @pl.when(step * BATCH < count)
    def _():
        parts = []
        for j in range(BATCH):
            s = step * BATCH + j
            r0 = pl.multiple_of(rows_ref[s] * tile, tile)
            c0 = pl.multiple_of(cols_ref[s] * tile, tile)
            xs = x_ref[pl.ds(r0, tile), :].astype(jnp.bfloat16)
            ys = y_ref[pl.ds(c0, tile), :]
            vals = v_ref[j].astype(jnp.float32)
            if want_rows:
                pred = lax.dot_general(xs, ys, (((1,), (1,)), ((), ())), preferred_element_type=jnp.float32)
                slope = jnp.where(s < count, jnp.clip(pred - vals, -huber_delta, huber_delta), 0.0).astype(jnp.bfloat16)
                parts.append((r0, jnp.dot(slope, ys, preferred_element_type=jnp.float32)))
            else:
                pred_t = lax.dot_general(ys, xs, (((1,), (1,)), ((), ())), preferred_element_type=jnp.float32)
                slope_t = jnp.where(s < count, jnp.clip(pred_t - vals, -huber_delta, huber_delta), 0.0).astype(jnp.bfloat16)
                parts.append((c0, jnp.dot(slope_t, xs, preferred_element_type=jnp.float32)))
        for o0, contrib in parts:
            acc_ref[pl.ds(o0, tile), :] += contrib

    @pl.when(step == pl.num_programs(0) - 1)
    def _():
        out_ref[...] = acc_ref[...].astype(out_ref.dtype)


def sweep(want_rows, xb, yb, values, rows_index, cols_index, filled, link):
    slots, tile, _ = values.shape
    segments = xb.shape[0] if want_rows else yb.shape[0]
    rank = xb.shape[1]
    batches = slots // BATCH

    def v_map(i, rows_ref, cols_ref, cnt_ref):
        last = jnp.maximum(cnt_ref[0] - 1, 0) // BATCH
        return (jnp.minimum(i, last), 0, 0)

    grid_spec = pltpu.PrefetchScalarGridSpec(
        num_scalar_prefetch=3,
        grid=(batches,),
        in_specs=[
            pl.BlockSpec(memory_space=pltpu.VMEM),
            pl.BlockSpec(memory_space=pltpu.VMEM),
            pl.BlockSpec((BATCH, tile, tile), v_map),
        ],
        out_specs=pl.BlockSpec((segments, rank), lambda i, *_: (0, 0)),
        scratch_shapes=[pltpu.VMEM((segments, rank), jnp.float32)],
    )
    flops = 4 * slots * tile * tile * rank
    cost = pl.CostEstimate(
        flops=flops,
        transcendentals=0,
        bytes_accessed=values.size * 2 + xb.size * xb.dtype.itemsize + yb.size * 2 + segments * rank * 2,
    )
    return pl.pallas_call(
        functools.partial(sweep_kernel, want_rows, tile),
        grid_spec=grid_spec,
        out_shape=jax.ShapeDtypeStruct((segments, rank), link),
        compiler_params=pltpu.CompilerParams(
            dimension_semantics=("arbitrary",),
            vmem_limit_bytes=60 * 1024 * 1024,
        ),
        cost_estimate=cost,
    )(rows_index, cols_index, filled, xb, yb, values)


def shards(x_rows, y_cols, tile_values, tile_row, tile_col, tile_count):
    slots = tile_row.shape[-1]
    tile = tile_values.shape[-1]
    yb = lax.all_gather(y_cols.astype(jnp.bfloat16), "wide", axis=0, tiled=True)
    values = tile_values.reshape(slots, tile, tile)
    rows_index = tile_row.reshape(slots)
    cols_index = tile_col.reshape(slots)
    filled = tile_count.reshape(1)

    rows_here = x_rows.shape[0] // lax.axis_size("narrow")
    first = lax.axis_index("narrow") * rows_here
    level = step_rows * penalty

    partial_rows = sweep(True, x_rows.astype(jnp.bfloat16), yb, values, rows_index, cols_index, filled, jnp.float32)
    grad_x = lax.psum_scatter(partial_rows, "narrow", scatter_dimension=0, tiled=True)
    x_mine = shrink(lax.dynamic_slice_in_dim(x_rows, first, rows_here, 0) - step_rows * grad_x, level)
    xb = lax.all_gather(x_mine.astype(jnp.bfloat16), "narrow", axis=0, tiled=True)

    partial_rows = sweep(True, xb, yb, values, rows_index, cols_index, filled, jnp.float32)
    grad_x = lax.psum_scatter(partial_rows, "narrow", scatter_dimension=0, tiled=True)
    x_mine = shrink(x_mine - step_rows * grad_x, level)
    upper = x_mine.astype(jnp.bfloat16)
    lower = (x_mine - upper.astype(jnp.float32)).astype(jnp.bfloat16)
    xb = lax.all_gather(upper, "narrow", axis=0, tiled=True)
    lower_all = lax.all_gather(lower, "narrow", axis=0, tiled=True)

    values_t = jnp.swapaxes(values, 1, 2)
    partial_cols = sweep(False, xb, yb, values_t, rows_index, cols_index, filled, jnp.bfloat16)
    grad_y = lax.psum_scatter(partial_cols, "wide", scatter_dimension=0, tiled=True).astype(jnp.float32)
    x_out = xb.astype(jnp.float32) + lower_all.astype(jnp.float32)
    return (x_out, y_cols - step_columns * grad_y)


def solution(mesh):
    placed = (
        P("wide", None),
        P(("wide", "narrow"), None),
        P("wide", "narrow", None, None, None),
        P("wide", "narrow", None),
        P("wide", "narrow", None),
        P("wide", "narrow"),
    )
    return jax.shard_map(
        shards,
        mesh=mesh,
        in_specs=placed,
        out_specs=(P("wide", None), P(("wide", "narrow"), None)),
        check_vma=False,
    )
```

```python
import functools

import jax
import jax.numpy as jnp
from jax import lax
from jax.experimental import pallas as pl
from jax.experimental.pallas import tpu as pltpu
from jax.sharding import PartitionSpec as P

huber_delta = 1.0
step_rows = 0.008
penalty = 3.0
step_columns = 0.012

BATCH = 64


def shrink(value, level):
    return jnp.sign(value) * jnp.maximum(jnp.abs(value) - level, 0.0)


def sweep_kernel(want_rows, echo, tile, rows_ref, cols_ref, cnt_ref, x_ref, y_ref, v_ref, *rest):
    if echo:
        out_ref, echo_ref, acc_ref = rest
    else:
        out_ref, acc_ref = rest[-2:]
    step = pl.program_id(0)
    count = cnt_ref[0]

    @pl.when(step == 0)
    def _():
        acc_ref[...] = jnp.zeros_like(acc_ref)
        if echo:
            echo_ref[...] = x_ref[...]

    @pl.when(step * BATCH < count)
    def _():
        parts = []
        for j in range(BATCH):
            s = step * BATCH + j
            r0 = pl.multiple_of(rows_ref[s] * tile, tile)
            c0 = pl.multiple_of(cols_ref[s] * tile, tile)
            xs = x_ref[pl.ds(r0, tile), :].astype(jnp.bfloat16)
            ys = y_ref[pl.ds(c0, tile), :]
            vals = v_ref[j].astype(jnp.float32)
            if want_rows:
                pred = lax.dot_general(xs, ys, (((1,), (1,)), ((), ())), preferred_element_type=jnp.float32)
                slope = jnp.where(s < count, jnp.clip(pred - vals, -huber_delta, huber_delta), 0.0).astype(jnp.bfloat16)
                parts.append((r0, jnp.dot(slope, ys, preferred_element_type=jnp.float32)))
            else:
                pred_t = lax.dot_general(ys, xs, (((1,), (1,)), ((), ())), preferred_element_type=jnp.float32)
                slope_t = jnp.where(s < count, jnp.clip(pred_t - vals, -huber_delta, huber_delta), 0.0).astype(jnp.bfloat16)
                parts.append((c0, jnp.dot(slope_t, xs, preferred_element_type=jnp.float32)))
        for o0, contrib in parts:
            acc_ref[pl.ds(o0, tile), :] += contrib

    @pl.when(step == pl.num_programs(0) - 1)
    def _():
        out_ref[...] = acc_ref[...].astype(out_ref.dtype)


def sweep(want_rows, xb, yb, values, rows_index, cols_index, filled, link, echo=False, hold=None):
    slots, tile, _ = values.shape
    segments = xb.shape[0] if want_rows else yb.shape[0]
    rank = xb.shape[1]
    batches = slots // BATCH

    def v_map(i, rows_ref, cols_ref, cnt_ref):
        last = jnp.maximum(cnt_ref[0] - 1, 0) // BATCH
        return (jnp.minimum(i, last), 0, 0)

    grid_spec = pltpu.PrefetchScalarGridSpec(
        num_scalar_prefetch=3,
        grid=(batches,),
        in_specs=[
            pl.BlockSpec(memory_space=pltpu.VMEM),
            pl.BlockSpec(memory_space=pltpu.VMEM),
            pl.BlockSpec((BATCH, tile, tile), v_map),
        ]
        + ([pl.BlockSpec(memory_space=pl.ANY)] if hold is not None else []),
        out_specs=[pl.BlockSpec((segments, rank), lambda i, *_: (0, 0))]
        + ([pl.BlockSpec(xb.shape, lambda i, *_: (0, 0))] if echo else []),
        scratch_shapes=[pltpu.VMEM((segments, rank), jnp.float32)],
    )
    flops = 4 * slots * tile * tile * rank
    cost = pl.CostEstimate(
        flops=flops,
        transcendentals=0,
        bytes_accessed=values.size * 2 + xb.size * xb.dtype.itemsize + yb.size * 2 + segments * rank * 2,
    )
    outs = pl.pallas_call(
        functools.partial(sweep_kernel, want_rows, echo, tile),
        grid_spec=grid_spec,
        out_shape=[jax.ShapeDtypeStruct((segments, rank), link)]
        + ([jax.ShapeDtypeStruct(xb.shape, xb.dtype)] if echo else []),
        compiler_params=pltpu.CompilerParams(
            dimension_semantics=("arbitrary",),
            vmem_limit_bytes=60 * 1024 * 1024,
        ),
        cost_estimate=cost,
    )(rows_index, cols_index, filled, xb, yb, values, *([] if hold is None else [hold]))
    return outs if echo else outs[0]


def shards(x_rows, y_cols, tile_values, tile_row, tile_col, tile_count):
    slots = tile_row.shape[-1]
    tile = tile_values.shape[-1]
    yb = lax.all_gather(y_cols.astype(jnp.bfloat16), "wide", axis=0, tiled=True)
    values = tile_values.reshape(slots, tile, tile)
    rows_index = tile_row.reshape(slots)
    cols_index = tile_col.reshape(slots)
    filled = tile_count.reshape(1)

    rows_here = x_rows.shape[0] // lax.axis_size("narrow")
    first = lax.axis_index("narrow") * rows_here
    level = step_rows * penalty

    values_t = jnp.swapaxes(values, 1, 2)
    partial_rows = sweep(True, x_rows.astype(jnp.bfloat16), yb, values, rows_index, cols_index, filled, jnp.float32, hold=values_t)
    grad_x = lax.psum_scatter(partial_rows, "narrow", scatter_dimension=0, tiled=True)
    x_mine = shrink(lax.dynamic_slice_in_dim(x_rows, first, rows_here, 0) - step_rows * grad_x, level)
    xb = lax.all_gather(x_mine.astype(jnp.bfloat16), "narrow", axis=0, tiled=True)

    partial_rows = sweep(True, xb, yb, values, rows_index, cols_index, filled, jnp.float32)
    grad_x = lax.psum_scatter(partial_rows, "narrow", scatter_dimension=0, tiled=True)
    x_mine = shrink(x_mine - step_rows * grad_x, level)
    x_now = lax.all_gather(x_mine, "narrow", axis=0, tiled=True)

    partial_cols, x_out = sweep(False, x_now, yb, values_t, rows_index, cols_index, filled, jnp.bfloat16, echo=True)
    grad_y = lax.psum_scatter(partial_cols, "wide", scatter_dimension=0, tiled=True).astype(jnp.float32)
    return (x_out, y_cols - step_columns * grad_y)


def solution(mesh):
    placed = (
        P("wide", None),
        P(("wide", "narrow"), None),
        P("wide", "narrow", None, None, None),
        P("wide", "narrow", None),
        P("wide", "narrow", None),
        P("wide", "narrow"),
    )
    return jax.shard_map(
        shards,
        mesh=mesh,
        in_specs=placed,
        out_specs=(P("wide", None), P(("wide", "narrow"), None)),
        check_vma=False,
    )
```

```python
import functools

import jax
import jax.numpy as jnp
from jax import lax
from jax.experimental import pallas as pl
from jax.experimental.pallas import tpu as pltpu
from jax.sharding import PartitionSpec as P

huber_delta = 1.0
step_rows = 0.008
penalty = 3.0
step_columns = 0.012

BATCH = 64


def shrink(value, level):
    return jnp.sign(value) * jnp.maximum(jnp.abs(value) - level, 0.0)


def sweep_kernel(want_rows, echo, tile, rows_ref, cols_ref, cnt_ref, x_ref, y_ref, v_ref, *rest):
    if echo:
        out_ref, echo_ref, acc_ref, xbuf = rest
    else:
        out_ref, acc_ref = rest[-2:]
        xbuf = x_ref
    step = pl.program_id(0)
    count = cnt_ref[0]

    @pl.when(step == 0)
    def _():
        acc_ref[...] = jnp.zeros_like(acc_ref)
        if echo:
            echo_ref[...] = x_ref[...]
            xbuf[...] = x_ref[...].astype(jnp.bfloat16)

    @pl.when(step * BATCH < count)
    def _():
        parts = []
        for j in range(BATCH):
            s = step * BATCH + j
            r0 = pl.multiple_of(rows_ref[s] * tile, tile)
            c0 = pl.multiple_of(cols_ref[s] * tile, tile)
            xs = xbuf[pl.ds(r0, tile), :]
            ys = y_ref[pl.ds(c0, tile), :]
            vals = v_ref[j].astype(jnp.float32)
            if want_rows:
                pred = lax.dot_general(xs, ys, (((1,), (1,)), ((), ())), preferred_element_type=jnp.float32)
                slope = jnp.where(s < count, jnp.clip(pred - vals, -huber_delta, huber_delta), 0.0).astype(jnp.bfloat16)
                parts.append((r0, jnp.dot(slope, ys, preferred_element_type=jnp.float32)))
            else:
                pred_t = lax.dot_general(ys, xs, (((1,), (1,)), ((), ())), preferred_element_type=jnp.float32)
                slope_t = jnp.where(s < count, jnp.clip(pred_t - vals, -huber_delta, huber_delta), 0.0).astype(jnp.bfloat16)
                parts.append((c0, jnp.dot(slope_t, xs, preferred_element_type=jnp.float32)))
        for o0, contrib in parts:
            acc_ref[pl.ds(o0, tile), :] += contrib

    @pl.when(step == pl.num_programs(0) - 1)
    def _():
        out_ref[...] = acc_ref[...].astype(out_ref.dtype)


def sweep(want_rows, xb, yb, values, rows_index, cols_index, filled, link, echo=False, hold=None):
    slots, tile, _ = values.shape
    segments = xb.shape[0] if want_rows else yb.shape[0]
    rank = xb.shape[1]
    batches = slots // BATCH

    def v_map(i, rows_ref, cols_ref, cnt_ref):
        last = jnp.maximum(cnt_ref[0] - 1, 0) // BATCH
        return (jnp.minimum(i, last), 0, 0)

    grid_spec = pltpu.PrefetchScalarGridSpec(
        num_scalar_prefetch=3,
        grid=(batches,),
        in_specs=[
            pl.BlockSpec(memory_space=pltpu.VMEM),
            pl.BlockSpec(memory_space=pltpu.VMEM),
            pl.BlockSpec((BATCH, tile, tile), v_map),
        ]
        + ([pl.BlockSpec(memory_space=pl.ANY)] if hold is not None else []),
        out_specs=[pl.BlockSpec((segments, rank), lambda i, *_: (0, 0))]
        + ([pl.BlockSpec(xb.shape, lambda i, *_: (0, 0))] if echo else []),
        scratch_shapes=[pltpu.VMEM((segments, rank), jnp.float32)]
        + ([pltpu.VMEM(xb.shape, jnp.bfloat16)] if echo else []),
    )
    flops = 4 * slots * tile * tile * rank
    cost = pl.CostEstimate(
        flops=flops,
        transcendentals=0,
        bytes_accessed=values.size * 2 + xb.size * xb.dtype.itemsize + yb.size * 2 + segments * rank * 2,
    )
    outs = pl.pallas_call(
        functools.partial(sweep_kernel, want_rows, echo, tile),
        grid_spec=grid_spec,
        out_shape=[jax.ShapeDtypeStruct((segments, rank), link)]
        + ([jax.ShapeDtypeStruct(xb.shape, xb.dtype)] if echo else []),
        compiler_params=pltpu.CompilerParams(
            dimension_semantics=("arbitrary",),
            vmem_limit_bytes=64000000,
        ),
        cost_estimate=cost,
    )(rows_index, cols_index, filled, xb, yb, values, *([] if hold is None else [hold]))
    return outs if echo else outs[0]


def shards(x_rows, y_cols, tile_values, tile_row, tile_col, tile_count):
    slots = tile_row.shape[-1]
    tile = tile_values.shape[-1]
    yb = lax.all_gather(y_cols.astype(jnp.bfloat16), "wide", axis=0, tiled=True)
    values = tile_values.reshape(slots, tile, tile)
    rows_index = tile_row.reshape(slots)
    cols_index = tile_col.reshape(slots)
    filled = tile_count.reshape(1)

    rows_here = x_rows.shape[0] // lax.axis_size("narrow")
    first = lax.axis_index("narrow") * rows_here
    level = step_rows * penalty

    values_t = jnp.swapaxes(values, 1, 2)
    partial_rows = sweep(True, x_rows.astype(jnp.bfloat16), yb, values, rows_index, cols_index, filled, jnp.float32, hold=values_t)
    grad_x = lax.psum_scatter(partial_rows, "narrow", scatter_dimension=0, tiled=True)
    x_mine = shrink(lax.dynamic_slice_in_dim(x_rows, first, rows_here, 0) - step_rows * grad_x, level)
    xb = lax.all_gather(x_mine.astype(jnp.bfloat16), "narrow", axis=0, tiled=True)

    partial_rows = sweep(True, xb, yb, values, rows_index, cols_index, filled, jnp.float32)
    grad_x = lax.psum_scatter(partial_rows, "narrow", scatter_dimension=0, tiled=True)
    x_mine = shrink(x_mine - step_rows * grad_x, level)
    x_now = lax.all_gather(x_mine, "narrow", axis=0, tiled=True)

    partial_cols, x_out = sweep(False, x_now, yb, values_t, rows_index, cols_index, filled, jnp.bfloat16, echo=True)
    grad_y = lax.psum_scatter(partial_cols, "wide", scatter_dimension=0, tiled=True).astype(jnp.float32)
    return (x_out, y_cols - step_columns * grad_y)


def solution(mesh):
    placed = (
        P("wide", None),
        P(("wide", "narrow"), None),
        P("wide", "narrow", None, None, None),
        P("wide", "narrow", None),
        P("wide", "narrow", None),
        P("wide", "narrow"),
    )
    return jax.shard_map(
        shards,
        mesh=mesh,
        in_specs=placed,
        out_specs=(P("wide", None), P(("wide", "narrow"), None)),
        check_vma=False,
    )
```

```python
import functools

import jax
import jax.numpy as jnp
from jax import lax
from jax.experimental import pallas as pl
from jax.experimental.pallas import tpu as pltpu
from jax.sharding import PartitionSpec as P

huber_delta = 1.0
step_rows = 0.008
penalty = 3.0
step_columns = 0.012

BATCH = 64


def shrink(value, level):
    return jnp.sign(value) * jnp.maximum(jnp.abs(value) - level, 0.0)


def sweep_kernel(want_rows, echo, tile, rows_ref, cols_ref, cnt_ref, x_ref, y_ref, v_ref, *rest):
    if echo:
        out_ref, echo_ref, acc_ref, xbuf = rest
    else:
        out_ref, acc_ref = rest[-2:]
        xbuf = x_ref
    step = pl.program_id(0)
    count = cnt_ref[0]

    @pl.when(step == 0)
    def _():
        acc_ref[...] = jnp.zeros_like(acc_ref)
        if echo:
            echo_ref[...] = x_ref[...]
            xbuf[...] = x_ref[...].astype(jnp.bfloat16)

    def run(masked):
        parts = []
        for j in range(BATCH):
            s = step * BATCH + j
            r0 = pl.multiple_of(rows_ref[s] * tile, tile)
            c0 = pl.multiple_of(cols_ref[s] * tile, tile)
            xs = xbuf[pl.ds(r0, tile), :]
            ys = y_ref[pl.ds(c0, tile), :]
            vals = v_ref[j].astype(jnp.float32)
            if want_rows:
                pred = lax.dot_general(xs, ys, (((1,), (1,)), ((), ())), preferred_element_type=jnp.float32)
            else:
                pred = lax.dot_general(ys, xs, (((1,), (1,)), ((), ())), preferred_element_type=jnp.float32)
            slope = jnp.clip(pred - vals, -huber_delta, huber_delta)
            if masked:
                slope = jnp.where(s < count, slope, 0.0)
            slope = slope.astype(jnp.bfloat16)
            if want_rows:
                parts.append((r0, jnp.dot(slope, ys, preferred_element_type=jnp.float32)))
            else:
                parts.append((c0, jnp.dot(slope, xs, preferred_element_type=jnp.float32)))
        for o0, contrib in parts:
            acc_ref[pl.ds(o0, tile), :] += contrib

    full = (step + 1) * BATCH <= count

    @pl.when(full)
    def _():
        run(False)

    @pl.when(jnp.logical_and(jnp.logical_not(full), step * BATCH < count))
    def _():
        run(True)

    @pl.when(step == pl.num_programs(0) - 1)
    def _():
        out_ref[...] = acc_ref[...].astype(out_ref.dtype)


def sweep(want_rows, xb, yb, values, rows_index, cols_index, filled, link, echo=False, hold=None):
    slots, tile, _ = values.shape
    segments = xb.shape[0] if want_rows else yb.shape[0]
    rank = xb.shape[1]
    batches = slots // BATCH

    def v_map(i, rows_ref, cols_ref, cnt_ref):
        last = jnp.maximum(cnt_ref[0] - 1, 0) // BATCH
        return (jnp.minimum(i, last), 0, 0)

    grid_spec = pltpu.PrefetchScalarGridSpec(
        num_scalar_prefetch=3,
        grid=(batches,),
        in_specs=[
            pl.BlockSpec(memory_space=pltpu.VMEM),
            pl.BlockSpec(memory_space=pltpu.VMEM),
            pl.BlockSpec((BATCH, tile, tile), v_map),
        ]
        + ([pl.BlockSpec(memory_space=pl.ANY)] if hold is not None else []),
        out_specs=[pl.BlockSpec((segments, rank), lambda i, *_: (0, 0))]
        + ([pl.BlockSpec(xb.shape, lambda i, *_: (0, 0))] if echo else []),
        scratch_shapes=[pltpu.VMEM((segments, rank), jnp.float32)]
        + ([pltpu.VMEM(xb.shape, jnp.bfloat16)] if echo else []),
    )
    flops = 4 * slots * tile * tile * rank
    cost = pl.CostEstimate(
        flops=flops,
        transcendentals=0,
        bytes_accessed=values.size * 2 + xb.size * xb.dtype.itemsize + yb.size * 2 + segments * rank * 2,
    )
    outs = pl.pallas_call(
        functools.partial(sweep_kernel, want_rows, echo, tile),
        grid_spec=grid_spec,
        out_shape=[jax.ShapeDtypeStruct((segments, rank), link)]
        + ([jax.ShapeDtypeStruct(xb.shape, xb.dtype)] if echo else []),
        compiler_params=pltpu.CompilerParams(
            dimension_semantics=("arbitrary",),
            vmem_limit_bytes=64000000,
        ),
        cost_estimate=cost,
    )(rows_index, cols_index, filled, xb, yb, values, *([] if hold is None else [hold]))
    return outs if echo else outs[0]


def shards(x_rows, y_cols, tile_values, tile_row, tile_col, tile_count):
    slots = tile_row.shape[-1]
    tile = tile_values.shape[-1]
    yb = lax.all_gather(y_cols.astype(jnp.bfloat16), "wide", axis=0, tiled=True)
    values = tile_values.reshape(slots, tile, tile)
    rows_index = tile_row.reshape(slots)
    cols_index = tile_col.reshape(slots)
    filled = tile_count.reshape(1)

    rows_here = x_rows.shape[0] // lax.axis_size("narrow")
    first = lax.axis_index("narrow") * rows_here
    level = step_rows * penalty

    values_t = jnp.swapaxes(values, 1, 2)
    partial_rows = sweep(True, x_rows.astype(jnp.bfloat16), yb, values, rows_index, cols_index, filled, jnp.float32, hold=values_t)
    grad_x = lax.psum_scatter(partial_rows, "narrow", scatter_dimension=0, tiled=True)
    x_mine = shrink(lax.dynamic_slice_in_dim(x_rows, first, rows_here, 0) - step_rows * grad_x, level)
    xb = lax.all_gather(x_mine.astype(jnp.bfloat16), "narrow", axis=0, tiled=True)

    partial_rows = sweep(True, xb, yb, values, rows_index, cols_index, filled, jnp.float32)
    grad_x = lax.psum_scatter(partial_rows, "narrow", scatter_dimension=0, tiled=True)
    x_mine = shrink(x_mine - step_rows * grad_x, level)
    x_now = lax.all_gather(x_mine, "narrow", axis=0, tiled=True)

    partial_cols, x_out = sweep(False, x_now, yb, values_t, rows_index, cols_index, filled, jnp.bfloat16, echo=True)
    grad_y = lax.psum_scatter(partial_cols, "wide", scatter_dimension=0, tiled=True).astype(jnp.float32)
    return (x_out, y_cols - step_columns * grad_y)


def solution(mesh):
    placed = (
        P("wide", None),
        P(("wide", "narrow"), None),
        P("wide", "narrow", None, None, None),
        P("wide", "narrow", None),
        P("wide", "narrow", None),
        P("wide", "narrow"),
    )
    return jax.shard_map(
        shards,
        mesh=mesh,
        in_specs=placed,
        out_specs=(P("wide", None), P(("wide", "narrow"), None)),
        check_vma=False,
    )
```
